768 devices in a mesh: dp: 24 (over x, z_hi, core), section: 8 (over y), mp: 4 (over z_lo).
Axes of the slice: x: 4, y: 8, z: 12 (z_hi: 3, z_lo: 4; z = z_hi * 4 + z_lo), core: 2. Of those that a mesh axis runs over, the one named last changes fastest.
Arguments:
- patch_features_window: bfloat16 [768, 729, 1152], P(('dp', 'section', 'mp')), may hold values from -2048 to 2048
- probe_request_heads: bfloat16 [1152], replicated, may hold values from -6 to 6
- lookup_projection: bfloat16 [1152, 1152], replicated, may hold values from -0.1875 to 0.1875
- content_projection: bfloat16 [1152, 1152], replicated, may hold values from -0.1875 to 0.1875
- final_projection: bfloat16 [1152, 1152], replicated, may hold values from -0.1875 to 0.1875
- prior_picture_entries: bfloat16 [23808, 1152], P(('dp', 'section', 'mp')), may hold values from -6 to 6
- caption_features: bfloat16 [24576, 1152], P(('dp', 'section', 'mp')), may hold values from -0.1875 to 0.1875
- partner_indices: int32 [24576], replicated, may hold values from 0 to 24575, each once
- score_scale_param: float32 [1], replicated, may hold values from 5 to 20
- score_shift: float32 [1], replicated, may hold values from -7.5 to -5.5
Outputs:
- losses: float32 [24576], P(('dp', 'section', 'mp'))
- text_grad: float32 [24576, 1152], P(('dp', 'section', 'mp'))
The draws below stay inside these ranges and needn't reach their ends.
Inputs may be any that keep to these rules, and one draw needn't show every extreme that they name: `partner_indices`: every text is the positive partner of exactly one image.
All inputs are finite; a program needn't handle non-finite values.
Results may differ from the reference program's by a relative error of at most 0.0046.
Values may be sent and summed in bfloat16 or wider, within the bound.
No kernel may reach another device: no remote copies, remote signals or barrier semaphores. Data moves between devices by JAX's collectives and lax.ppermute only.
A program may use at most 64 MiB of HBM per device.

```python
import math
import jax
import jax.numpy as jnp
from jax import lax

D = 1152
HEADS = 16
HD = 72
P_SIZE = 729
ROWS = 32
IMAGES = 768
BATCH = 24576
PREV = 23808


def draw_patch_features_window(key, part):
    base_key = jax.random.fold_in(key, 0)
    whole = jnp.clip(jax.random.normal(base_key, (IMAGES, P_SIZE, D), jnp.float32), -6.0, 6.0)
    return whole.astype(jnp.bfloat16)


def shard_levels(stream_key, extent, cuts, least, largest):
    def one(axis_at, shards_of):
        steps = jax.random.uniform(jax.random.fold_in(jax.random.fold_in(stream_key, 6), axis_at), (shards_of,), jnp.float32, least / len(cuts), largest / len(cuts))
        return jnp.repeat(jnp.exp(steps), extent[axis_at] // shards_of).reshape((-1,) + (1,) * (len(extent) - axis_at - 1))

    factor_of = one(*cuts[0])
    for cut in cuts[1:]:
        factor_of = factor_of * one(*cut)
    return factor_of


def centred(own_key, shape, spread, limit, cuts=(), kind=jnp.bfloat16):
    loudness = shard_levels(own_key, shape, cuts, -0.22, 0.18) if cuts else 1.0
    drawn = jax.random.normal(own_key, shape, jnp.float32) * spread * loudness
    return jnp.minimum(jnp.maximum(drawn, -limit), limit).astype(kind)


def setup_inputs(seed: int = 0) -> dict:
    arg_keys = jax.random.split(jax.random.key(seed), 11)
    return {
        "patch_features_window": draw_patch_features_window(jax.random.fold_in(arg_keys[10], 71), 0),
        "probe_request_heads": centred(arg_keys[1], (D,), 1.0, 6.0),
        "lookup_projection": centred(arg_keys[2], (D, D), D ** -0.5, 0.1875),
        "content_projection": centred(arg_keys[3], (D, D), D ** -0.5, 0.1875),
        "final_projection": centred(arg_keys[4], (D, D), D ** -0.5, 0.1875),
        "prior_picture_entries": centred(arg_keys[5], (PREV, D), 1.0, 6.0, ((0, 768),)),
        "caption_features": centred(arg_keys[6], (BATCH, D), D ** -0.5, 0.1875, ((0, 768),)),
        "partner_indices": jax.random.permutation(arg_keys[7], BATCH).astype(jnp.int32),
        "score_scale_param": jnp.clip(jnp.exp(jax.random.uniform(arg_keys[8], (1,), jnp.float32, math.log(5.0), math.log(20.0))), 5.0, 20.0),
        "score_shift": jnp.clip(jax.random.uniform(arg_keys[9], (1,), jnp.float32, -7.5, -5.5), -7.5, -5.5),
    }


def pool_image(patch_rows, probe_request_heads, lookup_projection, content_projection, final_projection):
    keys_wide = lookup_projection.astype(jnp.float32).reshape(D, HEADS, HD)
    query_wide = probe_request_heads.astype(jnp.float32).reshape(HEADS, HD)
    key_probe = (jnp.einsum('dhe,he->dh', keys_wide, query_wide) / math.sqrt(HD)).astype(jnp.bfloat16)
    scores = jnp.dot(patch_rows, key_probe, preferred_element_type=jnp.float32)
    highest = lax.optimization_barrier(jnp.max(scores, axis=0, keepdims=True))
    exponent = jnp.exp(scores - highest)
    weights = (exponent / lax.optimization_barrier(jnp.sum(exponent, axis=0, keepdims=True))).astype(jnp.bfloat16)
    pooled_patch = jnp.dot(weights.T, patch_rows, preferred_element_type=jnp.float32).astype(jnp.bfloat16)
    value_wide = content_projection.astype(jnp.float32).reshape(D, HEADS, HD)
    values = jnp.einsum('hd,dhe->he', pooled_patch.astype(jnp.float32), value_wide).astype(jnp.bfloat16).reshape(1, D)
    return jnp.dot(values, final_projection, preferred_element_type=jnp.float32).astype(jnp.bfloat16)

def normalize_rows(rows_in):
    widened = rows_in.astype(jnp.float32)
    inverse = lax.rsqrt(lax.optimization_barrier(jnp.sum(widened * widened, axis=1, keepdims=True)) + 1e-06)
    return (widened * inverse, inverse)

def reference(patch_features_window, probe_request_heads, lookup_projection, content_projection, final_projection, prior_picture_entries, caption_features, partner_indices, score_scale_param, score_shift):
    pooled = lax.map(lambda image: pool_image(image, probe_request_heads, lookup_projection, content_projection, final_projection), patch_features_window)
    earlier = prior_picture_entries.reshape(IMAGES, ROWS - 1, D)
    image_rows = jnp.concatenate([pooled, earlier], axis=1).reshape(BATCH, D)
    image_norm = normalize_rows(image_rows)[0].astype(jnp.bfloat16)
    text_unit, text_inverse = normalize_rows(caption_features)
    caption_magnitude = text_unit.astype(jnp.bfloat16)
    score_scaling = score_scale_param[0]
    starting_position = score_shift[0]
    span = 8 * ROWS
    image_parts = image_norm.reshape(BATCH // span, span, D)
    label_parts = partner_indices.reshape(BATCH // span, span)
    columns = jnp.arange(BATCH, dtype=jnp.int32)

    def visit(text_terms, part):
        picture_portion, label_part = part
        pair_scores = score_scaling * jnp.dot(picture_portion, caption_magnitude.T, preferred_element_type=jnp.float32) + starting_position
        matching_flag = label_part[:, None] == columns[None, :]
        row_losses = lax.optimization_barrier(jnp.sum(jax.nn.softplus(jnp.where(matching_flag, -pair_scores, pair_scores)), axis=1))
        sigmoid_derivatives = ((jax.nn.sigmoid(pair_scores) - matching_flag.astype(jnp.float32)) * score_scaling).astype(jnp.bfloat16)
        return (text_terms + jnp.dot(sigmoid_derivatives.T, picture_portion, preferred_element_type=jnp.float32), row_losses)
    text_terms, row_losses = lax.scan(visit, jnp.zeros((BATCH, D), jnp.float32), (image_parts, label_parts))
    along = lax.optimization_barrier(jnp.sum(text_unit * text_terms, axis=1, keepdims=True))
    text_grad = (text_terms - text_unit * along) * text_inverse
    return (row_losses.reshape(BATCH), text_grad)
```

```python
import math

import jax
import jax.numpy as jnp
from jax import lax
from jax.sharding import PartitionSpec as P

HEADS = 16
HD = 72


def pool_image(
    patch_rows, probe_request_heads, lookup_projection, content_projection, final_projection
):
    width = lookup_projection.shape[0]
    key_probe = jnp.einsum(
        "dhe,he->dh",
        lookup_projection.reshape(width, HEADS, HD),
        probe_request_heads.reshape(HEADS, HD),
        preferred_element_type=jnp.float32,
    )
    key_probe = (key_probe / math.sqrt(HD)).astype(jnp.bfloat16)
    scores = jnp.dot(patch_rows, key_probe, preferred_element_type=jnp.float32)
    highest = jnp.max(scores, axis=0, keepdims=True)
    exponent = jnp.exp(scores - highest)
    weights = (exponent / jnp.sum(exponent, axis=0, keepdims=True)).astype(jnp.bfloat16)
    pooled_patch = lax.dot_general(
        weights, patch_rows, (((0,), (0,)), ((), ())), preferred_element_type=jnp.float32
    ).astype(jnp.bfloat16)
    values = jnp.einsum(
        "hd,dhe->he",
        pooled_patch,
        content_projection.reshape(width, HEADS, HD),
        preferred_element_type=jnp.float32,
    )
    values = values.astype(jnp.bfloat16).reshape(1, width)
    return jnp.dot(values, final_projection, preferred_element_type=jnp.float32).astype(
        jnp.bfloat16
    )


def normalize_rows(rows_in):
    widened = rows_in.astype(jnp.float32)
    inverse = lax.rsqrt(jnp.sum(widened * widened, axis=1, keepdims=True) + 1e-06)
    return (widened * inverse, inverse)


def block_contributions(
    picture_tile,
    target_tile,
    device_portion_count,
    overall_column_indices,
    score_scaling,
    starting_position,
):
    pair_scores = (
        score_scaling
        * lax.dot_general(
            picture_tile,
            device_portion_count,
            (((1,), (1,)), ((), ())),
            preferred_element_type=jnp.float32,
        )
        + starting_position
    )
    matching_flag = target_tile[:, None] == overall_column_indices[None, :]
    row_losses = jnp.sum(
        jax.nn.softplus(jnp.where(matching_flag, -pair_scores, pair_scores)), axis=1
    )
    sigmoid_derivatives = (
        (jax.nn.sigmoid(pair_scores) - matching_flag.astype(jnp.float32)) * score_scaling
    ).astype(jnp.bfloat16)
    grad_terms = lax.dot_general(
        sigmoid_derivatives,
        picture_tile,
        (((0,), (0,)), ((), ())),
        preferred_element_type=jnp.float32,
    )
    return (row_losses, grad_terms)


def shift_ring(x, axis, size, step):
    return lax.ppermute(x, axis, [(i, (i + step) % size) for i in range(size)])


def ring_gather(x, axis, size):
    forward, backward = x, x
    arrived = {0: x}
    forward_steps = size // 2
    backward_steps = size - 1 - forward_steps
    for step in range(1, forward_steps + 1):
        forward = shift_ring(forward, axis, size, 1)
        arrived[(size - step) % size] = forward
        if step <= backward_steps:
            backward = shift_ring(backward, axis, size, -1)
            arrived[step] = backward
    return jnp.concatenate([arrived[d] for d in range(size)], axis=0)


def direct_scatter(x, axis, size):
    pos = lax.axis_index(axis)
    blocks = x.reshape(size, x.shape[0] // size, *x.shape[1:])
    total = lax.dynamic_index_in_dim(blocks, pos, 0, keepdims=False)
    for step in range(1, size):
        outgoing = lax.dynamic_index_in_dim(blocks, (pos + step) % size, 0, keepdims=False)
        total = total + shift_ring(outgoing, axis, size, step)
    return total


def local(
    patch_features_window,
    probe_request_heads,
    lookup_projection,
    content_projection,
    final_projection,
    prior_picture_entries,
    caption_features,
    partner_indices,
    score_scale_param,
    score_shift,
):
    row_count = caption_features.shape[0]
    prior_count = prior_picture_entries.shape[0]
    section_size = lax.axis_size("section")
    mp_size = lax.axis_size("mp")
    inner_size = section_size * mp_size
    section_pos = lax.axis_index("section")
    mp_pos = lax.axis_index("mp")
    inner_pos = section_pos * mp_size + mp_pos
    outer_pos = lax.axis_index(("x", "zh", "core"))
    x_size, zh_size, core_size = lax.axis_size("x"), lax.axis_size("zh"), lax.axis_size("core")
    outer_size = x_size * zh_size * core_size
    score_scaling = score_scale_param[0]
    starting_position = score_shift[0]

    text_unit, text_inverse = normalize_rows(caption_features)
    caption_magnitude = text_unit.astype(jnp.bfloat16)
    device_portion_count = lax.all_gather(caption_magnitude, ("x", "zh", "core"), axis=0, tiled=True)

    prior_norm = normalize_rows(prior_picture_entries)[0].astype(jnp.bfloat16)
    chunk_rows = row_count
    prior_norm = jnp.concatenate(
        [prior_norm, jnp.zeros((chunk_rows - prior_count, prior_norm.shape[1]), jnp.bfloat16)],
        axis=0,
    )
    prior_tile = ring_gather(ring_gather(prior_norm, "mp", mp_size), "section", section_size)

    pooled = pool_image(
        patch_features_window[0],
        probe_request_heads,
        lookup_projection,
        content_projection,
        final_projection,
    )
    pooled_norm = normalize_rows(pooled)[0].astype(jnp.bfloat16)
    pooled_tile = lax.all_to_all(
        jnp.broadcast_to(pooled_norm, (inner_size, pooled_norm.shape[1])),
        ("section", "mp"),
        0,
        0,
        tiled=True,
    )
    picture_tile = jnp.concatenate([prior_tile, pooled_tile], axis=0)

    group_labels = lax.dynamic_slice_in_dim(
        partner_indices, outer_pos * (inner_size * row_count), inner_size * row_count
    ).reshape(section_size, mp_size, row_count)
    ring_labels = jnp.roll(jnp.roll(group_labels, -section_pos, axis=0), -mp_pos, axis=1)
    prior_labels = jnp.concatenate(
        [
            ring_labels[:, :, 1 : 1 + prior_count],
            jnp.full((section_size, mp_size, chunk_rows - prior_count), -1, jnp.int32),
        ],
        axis=2,
    ).reshape(-1)
    pooled_labels = group_labels[:, :, 0].reshape(-1)
    target_tile = jnp.concatenate([prior_labels, pooled_labels])

    width = device_portion_count.shape[1]
    device_portion_count = (
        device_portion_count.reshape(x_size, zh_size, core_size, row_count, width)
        .transpose(2, 0, 1, 3, 4)
        .reshape(outer_size * row_count, width)
    )
    blocks = jnp.arange(outer_size, dtype=jnp.int32)
    block_core = blocks // (x_size * zh_size)
    block_x = blocks // zh_size % x_size
    block_zh = blocks % zh_size
    block_dp = block_x * (zh_size * core_size) + block_zh * core_size + block_core
    overall_column_indices = (
        (block_dp * inner_size + inner_pos)[:, None] * row_count
        + jnp.arange(row_count, dtype=jnp.int32)[None, :]
    ).reshape(-1)

    row_losses, grad_terms = block_contributions(
        picture_tile,
        target_tile,
        device_portion_count,
        overall_column_indices,
        score_scaling,
        starting_position,
    )
    prior_losses = row_losses[: inner_size * chunk_rows].reshape(section_size, mp_size, chunk_rows)
    prior_losses = jnp.roll(jnp.roll(prior_losses, section_pos, axis=0), mp_pos, axis=1)
    pooled_losses = row_losses[inner_size * chunk_rows :]
    loss_parts = jnp.concatenate(
        [pooled_losses[:, None], prior_losses.reshape(inner_size, chunk_rows)[:, :prior_count]],
        axis=1,
    )
    own_losses = jnp.sum(
        lax.all_to_all(loss_parts, ("section", "mp"), 0, 0, tiled=True), axis=0
    )

    own_terms = direct_scatter(
        direct_scatter(direct_scatter(grad_terms, "core", core_size), "x", x_size), "zh", zh_size
    )
    along = jnp.sum(text_unit * own_terms, axis=1, keepdims=True)
    text_grad = (own_terms - text_unit * along) * text_inverse
    return (own_losses, text_grad)


def solution(mesh):
    outer = mesh.shape["dp"]
    core_size = 2
    x_size = outer // (core_size * 3)
    fine_mesh = jax.sharding.Mesh(
        mesh.devices.reshape(x_size, 3, core_size, mesh.shape["section"], mesh.shape["mp"]),
        ("x", "zh", "core", "section", "mp"),
    )
    spread = ("x", "zh", "core", "section", "mp")
    placed = (
        P(spread, None, None),
        P(),
        P(),
        P(),
        P(),
        P(spread, None),
        P(spread, None),
        P(),
        P(),
        P(),
    )
    return jax.shard_map(
        local,
        mesh=fine_mesh,
        in_specs=placed,
        out_specs=(P(spread), P(spread, None)),
        check_vma=False,
    )
```

```python
import math

import jax
import jax.numpy as jnp
from jax import lax
from jax.sharding import PartitionSpec as P

HEADS = 16
HD = 72


def pool_image(
    patch_rows, probe_request_heads, lookup_projection, content_projection, final_projection
):
    width = lookup_projection.shape[0]
    head_of_column = jnp.arange(width, dtype=jnp.int32) // HD
    probe_blocks = jnp.where(
        head_of_column[:, None] == jnp.arange(HEADS, dtype=jnp.int32)[None, :],
        probe_request_heads[:, None],
        jnp.zeros((), probe_request_heads.dtype),
    )
    key_probe = jnp.dot(lookup_projection, probe_blocks, preferred_element_type=jnp.float32)
    key_probe = (key_probe / math.sqrt(HD)).astype(jnp.bfloat16)
    scores = jnp.dot(patch_rows, key_probe, preferred_element_type=jnp.float32)
    highest = jnp.max(scores, axis=0, keepdims=True)
    exponent = jnp.exp(scores - highest)
    weights = (exponent / jnp.sum(exponent, axis=0, keepdims=True)).astype(jnp.bfloat16)
    pooled_patch = lax.dot_general(
        weights, patch_rows, (((0,), (0,)), ((), ())), preferred_element_type=jnp.float32
    ).astype(jnp.bfloat16)
    every_head = jnp.dot(pooled_patch, content_projection, preferred_element_type=jnp.float32)
    values = jnp.sum(
        every_head.reshape(HEADS, HEADS, HD)
        * jnp.eye(HEADS, dtype=jnp.float32)[:, :, None],
        axis=1,
    )
    values = values.astype(jnp.bfloat16).reshape(1, width)
    return jnp.dot(values, final_projection, preferred_element_type=jnp.float32).astype(
        jnp.bfloat16
    )


def normalize_rows(rows_in):
    widened = rows_in.astype(jnp.float32)
    inverse = lax.rsqrt(jnp.sum(widened * widened, axis=1, keepdims=True) + 1e-06)
    return (widened * inverse, inverse)


def block_contributions(
    picture_tile,
    target_tile,
    device_portion_count,
    overall_column_indices,
    score_scaling,
    starting_position,
):
    pair_scores = (
        score_scaling
        * lax.dot_general(
            picture_tile,
            device_portion_count,
            (((1,), (1,)), ((), ())),
            preferred_element_type=jnp.float32,
        )
        + starting_position
    )
    matching_flag = target_tile[:, None] == overall_column_indices[None, :]
    row_losses = jnp.sum(
        jax.nn.softplus(jnp.where(matching_flag, -pair_scores, pair_scores)), axis=1
    )
    sigmoid_derivatives = (
        (jax.nn.sigmoid(pair_scores) - matching_flag.astype(jnp.float32)) * score_scaling
    ).astype(jnp.bfloat16)
    grad_terms = lax.dot_general(
        sigmoid_derivatives,
        picture_tile,
        (((0,), (0,)), ((), ())),
        preferred_element_type=jnp.float32,
    )
    return (row_losses, grad_terms)


def shift_ring(x, axis, size, step):
    return lax.ppermute(x, axis, [(i, (i + step) % size) for i in range(size)])


def ring_gather(x, axis, size):
    forward, backward = x, x
    arrived = {0: x}
    forward_steps = size // 2
    backward_steps = size - 1 - forward_steps
    for step in range(1, forward_steps + 1):
        forward = shift_ring(forward, axis, size, 1)
        arrived[(size - step) % size] = forward
        if step <= backward_steps:
            backward = shift_ring(backward, axis, size, -1)
            arrived[step] = backward
    return jnp.concatenate([arrived[d] for d in range(size)], axis=0)


def direct_scatter(x, axis, size):
    pos = lax.axis_index(axis)
    blocks = x.reshape(size, x.shape[0] // size, *x.shape[1:])
    total = lax.dynamic_index_in_dim(blocks, pos, 0, keepdims=False)
    for step in range(1, size):
        outgoing = lax.dynamic_index_in_dim(blocks, (pos + step) % size, 0, keepdims=False)
        total = total + shift_ring(outgoing, axis, size, step)
    return total


def local(
    patch_features_window,
    probe_request_heads,
    lookup_projection,
    content_projection,
    final_projection,
    prior_picture_entries,
    caption_features,
    partner_indices,
    score_scale_param,
    score_shift,
):
    row_count = caption_features.shape[0]
    prior_count = prior_picture_entries.shape[0]
    section_size = lax.axis_size("section")
    mp_size = lax.axis_size("mp")
    inner_size = section_size * mp_size
    section_pos = lax.axis_index("section")
    mp_pos = lax.axis_index("mp")
    inner_pos = section_pos * mp_size + mp_pos
    outer_pos = lax.axis_index(("x", "zh", "core"))
    x_size, zh_size, core_size = lax.axis_size("x"), lax.axis_size("zh"), lax.axis_size("core")
    outer_size = x_size * zh_size * core_size
    score_scaling = score_scale_param[0]
    starting_position = score_shift[0]

    text_unit, text_inverse = normalize_rows(caption_features)
    caption_magnitude = text_unit.astype(jnp.bfloat16)
    device_portion_count = lax.all_gather(caption_magnitude, ("x", "zh", "core"), axis=0, tiled=True)

    chunk_rows = row_count
    prior_norm = normalize_rows(
        jnp.pad(prior_picture_entries, ((0, chunk_rows - prior_count), (0, 0)))
    )[0].astype(jnp.bfloat16)
    prior_tile = ring_gather(ring_gather(prior_norm, "mp", mp_size), "section", section_size)

    pooled = pool_image(
        patch_features_window[0],
        probe_request_heads,
        lookup_projection,
        content_projection,
        final_projection,
    )
    pooled_norm = normalize_rows(pooled)[0].astype(jnp.bfloat16)
    pooled_tile = lax.all_to_all(
        jnp.broadcast_to(pooled_norm, (inner_size, pooled_norm.shape[1])),
        ("section", "mp"),
        0,
        0,
        tiled=True,
    )
    picture_tile = jnp.concatenate([prior_tile, pooled_tile], axis=0)

    group_labels = lax.dynamic_slice_in_dim(
        partner_indices, outer_pos * (inner_size * row_count), inner_size * row_count
    ).reshape(section_size, mp_size, row_count)
    ring_labels = jnp.roll(jnp.roll(group_labels, -section_pos, axis=0), -mp_pos, axis=1)
    prior_labels = jnp.concatenate(
        [
            ring_labels[:, :, 1 : 1 + prior_count],
            jnp.full((section_size, mp_size, chunk_rows - prior_count), -1, jnp.int32),
        ],
        axis=2,
    ).reshape(-1)
    pooled_labels = group_labels[:, :, 0].reshape(-1)
    target_tile = jnp.concatenate([prior_labels, pooled_labels])

    width = device_portion_count.shape[1]
    device_portion_count = (
        device_portion_count.reshape(x_size, zh_size, core_size, row_count, width)
        .transpose(2, 0, 1, 3, 4)
        .reshape(outer_size * row_count, width)
    )
    blocks = jnp.arange(outer_size, dtype=jnp.int32)
    block_core = blocks // (x_size * zh_size)
    block_x = blocks // zh_size % x_size
    block_zh = blocks % zh_size
    block_dp = block_x * (zh_size * core_size) + block_zh * core_size + block_core
    overall_column_indices = (
        (block_dp * inner_size + inner_pos)[:, None] * row_count
        + jnp.arange(row_count, dtype=jnp.int32)[None, :]
    ).reshape(-1)

    row_losses, grad_terms = block_contributions(
        picture_tile,
        target_tile,
        device_portion_count,
        overall_column_indices,
        score_scaling,
        starting_position,
    )
    prior_losses = row_losses[: inner_size * chunk_rows].reshape(section_size, mp_size, chunk_rows)
    prior_losses = jnp.roll(jnp.roll(prior_losses, section_pos, axis=0), mp_pos, axis=1)
    pooled_losses = row_losses[inner_size * chunk_rows :]
    loss_parts = jnp.concatenate(
        [pooled_losses[:, None], prior_losses.reshape(inner_size, chunk_rows)[:, :prior_count]],
        axis=1,
    )
    own_losses = jnp.sum(
        lax.all_to_all(loss_parts, ("section", "mp"), 0, 0, tiled=True), axis=0
    )

    own_terms = direct_scatter(
        direct_scatter(direct_scatter(grad_terms, "core", core_size), "x", x_size), "zh", zh_size
    )
    along = jnp.sum(text_unit * own_terms, axis=1, keepdims=True)
    text_grad = (own_terms - text_unit * along) * text_inverse
    return (own_losses, text_grad)


def solution(mesh):
    outer = mesh.shape["dp"]
    core_size = 2
    x_size = outer // (core_size * 3)
    fine_mesh = jax.sharding.Mesh(
        mesh.devices.reshape(x_size, 3, core_size, mesh.shape["section"], mesh.shape["mp"]),
        ("x", "zh", "core", "section", "mp"),
    )
    spread = ("x", "zh", "core", "section", "mp")
    placed = (
        P(spread, None, None),
        P(),
        P(),
        P(),
        P(),
        P(spread, None),
        P(spread, None),
        P(),
        P(),
        P(),
    )
    return jax.shard_map(
        local,
        mesh=fine_mesh,
        in_specs=placed,
        out_specs=(P(spread), P(spread, None)),
        check_vma=False,
    )
```

```python
import math

import jax
import jax.numpy as jnp
from jax import lax
from jax.sharding import PartitionSpec as P

HEADS = 16
HD = 72


def pool_image(
    patch_rows, probe_request_heads, lookup_projection, content_projection, final_projection
):
    width = lookup_projection.shape[0]
    head_of_column = jnp.arange(width, dtype=jnp.int32) // HD
    probe_blocks = jnp.where(
        head_of_column[:, None] == jnp.arange(HEADS, dtype=jnp.int32)[None, :],
        probe_request_heads[:, None],
        jnp.zeros((), probe_request_heads.dtype),
    )
    key_probe = jnp.dot(lookup_projection, probe_blocks, preferred_element_type=jnp.float32)
    key_probe = (key_probe / math.sqrt(HD)).astype(jnp.bfloat16)
    scores = jnp.dot(patch_rows, key_probe, preferred_element_type=jnp.float32)
    highest = jnp.max(scores, axis=0, keepdims=True)
    exponent = jnp.exp(scores - highest)
    weights = (exponent / jnp.sum(exponent, axis=0, keepdims=True)).astype(jnp.bfloat16)
    pooled_patch = lax.dot_general(
        weights, patch_rows, (((0,), (0,)), ((), ())), preferred_element_type=jnp.float32
    ).astype(jnp.bfloat16)
    every_head = jnp.dot(pooled_patch, content_projection, preferred_element_type=jnp.float32)
    values = jnp.sum(
        every_head.reshape(HEADS, HEADS, HD)
        * jnp.eye(HEADS, dtype=jnp.float32)[:, :, None],
        axis=1,
    )
    values = values.astype(jnp.bfloat16).reshape(1, width)
    return jnp.dot(values, final_projection, preferred_element_type=jnp.float32).astype(
        jnp.bfloat16
    )


def normalize_rows(rows_in):
    widened = rows_in.astype(jnp.float32)
    inverse = lax.rsqrt(jnp.sum(widened * widened, axis=1, keepdims=True) + 1e-06)
    return (widened * inverse, inverse)


def block_contributions(
    picture_tile,
    target_tile,
    device_portion_count,
    overall_column_indices,
    score_scaling,
    starting_position,
):
    pair_scores = (
        score_scaling
        * lax.dot_general(
            picture_tile,
            device_portion_count,
            (((1,), (1,)), ((), ())),
            preferred_element_type=jnp.float32,
        )
        + starting_position
    )
    matching_flag = target_tile[:, None] == overall_column_indices[None, :]
    row_losses = jnp.sum(
        jax.nn.softplus(jnp.where(matching_flag, -pair_scores, pair_scores)), axis=1
    )
    sigmoid_derivatives = (
        (jax.nn.sigmoid(pair_scores) - matching_flag.astype(jnp.float32)) * score_scaling
    ).astype(jnp.bfloat16)
    grad_terms = lax.dot_general(
        sigmoid_derivatives,
        picture_tile,
        (((0,), (0,)), ((), ())),
        preferred_element_type=jnp.float32,
    )
    return (row_losses, grad_terms)


def shift_ring(x, axis, size, step):
    return lax.ppermute(x, axis, [(i, (i + step) % size) for i in range(size)])


def ring_gather(x, axis, size, held=None, held_step=0):
    forward, backward = x, x
    arrived = {0: x}
    forward_steps = size // 2
    backward_steps = size - 1 - forward_steps
    for step in range(1, forward_steps + 1):
        if held is not None and step == held_step:
            forward, held = lax.optimization_barrier((forward, held))
        forward = shift_ring(forward, axis, size, 1)
        arrived[(size - step) % size] = forward
        if step <= backward_steps:
            backward = shift_ring(backward, axis, size, -1)
            arrived[step] = backward
    tile = jnp.concatenate([arrived[d] for d in range(size)], axis=0)
    return tile if held is None else (tile, held)


def direct_scatter(x, axis, size):
    pos = lax.axis_index(axis)
    blocks = x.reshape(size, x.shape[0] // size, *x.shape[1:])
    total = lax.dynamic_index_in_dim(blocks, pos, 0, keepdims=False)
    for step in range(1, size):
        outgoing = lax.dynamic_index_in_dim(blocks, (pos + step) % size, 0, keepdims=False)
        total = total + shift_ring(outgoing, axis, size, step)
    return total


def local(
    patch_features_window,
    probe_request_heads,
    lookup_projection,
    content_projection,
    final_projection,
    prior_picture_entries,
    caption_features,
    partner_indices,
    score_scale_param,
    score_shift,
):
    row_count = caption_features.shape[0]
    prior_count = prior_picture_entries.shape[0]
    section_size = lax.axis_size("section")
    mp_size = lax.axis_size("mp")
    inner_size = section_size * mp_size
    section_pos = lax.axis_index("section")
    mp_pos = lax.axis_index("mp")
    inner_pos = section_pos * mp_size + mp_pos
    outer_pos = lax.axis_index(("x", "zh", "core"))
    x_size, zh_size, core_size = lax.axis_size("x"), lax.axis_size("zh"), lax.axis_size("core")
    outer_size = x_size * zh_size * core_size
    score_scaling = score_scale_param[0]
    starting_position = score_shift[0]

    text_unit, text_inverse = normalize_rows(caption_features)
    caption_magnitude = text_unit.astype(jnp.bfloat16)
    device_portion_count = lax.all_gather(caption_magnitude, ("x", "zh", "core"), axis=0, tiled=True)

    chunk_rows = row_count
    prior_norm = normalize_rows(
        jnp.pad(prior_picture_entries, ((0, chunk_rows - prior_count), (0, 0)))
    )[0].astype(jnp.bfloat16)
    prior_tile, device_portion_count = ring_gather(
        ring_gather(prior_norm, "mp", mp_size),
        "section",
        section_size,
        held=device_portion_count,
        held_step=section_size // 2,
    )

    pooled = pool_image(
        patch_features_window[0],
        probe_request_heads,
        lookup_projection,
        content_projection,
        final_projection,
    )
    pooled_norm = normalize_rows(pooled)[0].astype(jnp.bfloat16)
    pooled_tile = lax.all_to_all(
        jnp.broadcast_to(pooled_norm, (inner_size, pooled_norm.shape[1])),
        ("section", "mp"),
        0,
        0,
        tiled=True,
    )
    picture_tile = jnp.concatenate([prior_tile, pooled_tile], axis=0)

    group_labels = lax.dynamic_slice_in_dim(
        partner_indices, outer_pos * (inner_size * row_count), inner_size * row_count
    ).reshape(section_size, mp_size, row_count)
    ring_labels = jnp.roll(jnp.roll(group_labels, -section_pos, axis=0), -mp_pos, axis=1)
    prior_labels = jnp.concatenate(
        [
            ring_labels[:, :, 1 : 1 + prior_count],
            jnp.full((section_size, mp_size, chunk_rows - prior_count), -1, jnp.int32),
        ],
        axis=2,
    ).reshape(-1)
    pooled_labels = group_labels[:, :, 0].reshape(-1)
    target_tile = jnp.concatenate([prior_labels, pooled_labels])

    width = device_portion_count.shape[1]
    device_portion_count = (
        device_portion_count.reshape(x_size, zh_size, core_size, row_count, width)
        .transpose(2, 0, 1, 3, 4)
        .reshape(outer_size * row_count, width)
    )
    blocks = jnp.arange(outer_size, dtype=jnp.int32)
    block_core = blocks // (x_size * zh_size)
    block_x = blocks // zh_size % x_size
    block_zh = blocks % zh_size
    block_dp = block_x * (zh_size * core_size) + block_zh * core_size + block_core
    overall_column_indices = (
        (block_dp * inner_size + inner_pos)[:, None] * row_count
        + jnp.arange(row_count, dtype=jnp.int32)[None, :]
    ).reshape(-1)

    row_losses, grad_terms = block_contributions(
        picture_tile,
        target_tile,
        device_portion_count,
        overall_column_indices,
        score_scaling,
        starting_position,
    )
    prior_losses = row_losses[: inner_size * chunk_rows].reshape(section_size, mp_size, chunk_rows)
    prior_losses = jnp.roll(jnp.roll(prior_losses, section_pos, axis=0), mp_pos, axis=1)
    pooled_losses = row_losses[inner_size * chunk_rows :]
    loss_parts = jnp.concatenate(
        [pooled_losses[:, None], prior_losses.reshape(inner_size, chunk_rows)[:, :prior_count]],
        axis=1,
    )
    own_losses = jnp.sum(
        lax.all_to_all(loss_parts, ("section", "mp"), 0, 0, tiled=True), axis=0
    )

    own_terms = direct_scatter(
        direct_scatter(direct_scatter(grad_terms, "core", core_size), "x", x_size), "zh", zh_size
    )
    along = jnp.sum(text_unit * own_terms, axis=1, keepdims=True)
    text_grad = (own_terms - text_unit * along) * text_inverse
    return (own_losses, text_grad)


def solution(mesh):
    outer = mesh.shape["dp"]
    core_size = 2
    x_size = outer // (core_size * 3)
    fine_mesh = jax.sharding.Mesh(
        mesh.devices.reshape(x_size, 3, core_size, mesh.shape["section"], mesh.shape["mp"]),
        ("x", "zh", "core", "section", "mp"),
    )
    spread = ("x", "zh", "core", "section", "mp")
    placed = (
        P(spread, None, None),
        P(),
        P(),
        P(),
        P(),
        P(spread, None),
        P(spread, None),
        P(),
        P(),
        P(),
    )
    return jax.shard_map(
        local,
        mesh=fine_mesh,
        in_specs=placed,
        out_specs=(P(spread), P(spread, None)),
        check_vma=False,
    )
```

```python
import math

import jax
import jax.numpy as jnp
from jax import lax
from jax.sharding import PartitionSpec as P

HEADS = 16
HD = 72


def pool_image(
    patch_rows, probe_request_heads, lookup_projection, content_projection, final_projection
):
    width = lookup_projection.shape[0]
    head_of_column = jnp.arange(width, dtype=jnp.int32) // HD
    probe_blocks = jnp.where(
        head_of_column[:, None] == jnp.arange(HEADS, dtype=jnp.int32)[None, :],
        probe_request_heads[:, None],
        jnp.zeros((), probe_request_heads.dtype),
    )
    key_probe = jnp.dot(lookup_projection, probe_blocks, preferred_element_type=jnp.float32)
    key_probe = (key_probe / math.sqrt(HD)).astype(jnp.bfloat16)
    scores = jnp.dot(patch_rows, key_probe, preferred_element_type=jnp.float32)
    highest = jnp.max(scores, axis=0, keepdims=True)
    exponent = jnp.exp(scores - highest)
    weights = (exponent / jnp.sum(exponent, axis=0, keepdims=True)).astype(jnp.bfloat16)
    pooled_patch = lax.dot_general(
        weights, patch_rows, (((0,), (0,)), ((), ())), preferred_element_type=jnp.float32
    ).astype(jnp.bfloat16)
    every_head = jnp.dot(pooled_patch, content_projection, preferred_element_type=jnp.float32)
    values = jnp.sum(
        every_head.reshape(HEADS, HEADS, HD)
        * jnp.eye(HEADS, dtype=jnp.float32)[:, :, None],
        axis=1,
    )
    values = values.astype(jnp.bfloat16).reshape(1, width)
    return jnp.dot(values, final_projection, preferred_element_type=jnp.float32).astype(
        jnp.bfloat16
    )


def normalize_rows(rows_in):
    widened = rows_in.astype(jnp.float32)
    inverse = lax.rsqrt(jnp.sum(widened * widened, axis=1, keepdims=True) + 1e-06)
    return (widened * inverse, inverse)


def block_contributions(
    picture_tile,
    target_tile,
    device_portion_count,
    overall_column_indices,
    score_scaling,
    starting_position,
):
    pair_scores = (
        score_scaling
        * lax.dot_general(
            picture_tile,
            device_portion_count,
            (((1,), (1,)), ((), ())),
            preferred_element_type=jnp.float32,
        )
        + starting_position
    )
    matching_flag = target_tile[:, None] == overall_column_indices[None, :]
    row_losses = jnp.sum(
        jax.nn.softplus(jnp.where(matching_flag, -pair_scores, pair_scores)), axis=1
    )
    sigmoid_derivatives = (
        (jax.nn.sigmoid(pair_scores) - matching_flag.astype(jnp.float32)) * score_scaling
    ).astype(jnp.bfloat16)
    grad_terms = lax.dot_general(
        sigmoid_derivatives,
        picture_tile,
        (((0,), (0,)), ((), ())),
        preferred_element_type=jnp.float32,
    )
    return (row_losses, grad_terms)


def shift_ring(x, axis, size, step):
    return lax.ppermute(x, axis, [(i, (i + step) % size) for i in range(size)])


def ring_gather(x, axis, size, held=None, held_step=0):
    forward, backward = x, x
    arrived = {0: x}
    forward_steps = size // 2
    backward_steps = size - 1 - forward_steps
    for step in range(1, forward_steps + 1):
        if held is not None and step == held_step:
            forward, held = lax.optimization_barrier((forward, held))
        forward = shift_ring(forward, axis, size, 1)
        arrived[(size - step) % size] = forward
        if step <= backward_steps:
            backward = shift_ring(backward, axis, size, -1)
            arrived[step] = backward
    tile = jnp.concatenate([arrived[d] for d in range(size)], axis=0)
    return tile if held is None else (tile, held)


def direct_scatter(x, axis, size):
    pos = lax.axis_index(axis)
    blocks = x.reshape(size, x.shape[0] // size, *x.shape[1:])
    total = lax.dynamic_index_in_dim(blocks, pos, 0, keepdims=False)
    for step in range(1, size):
        outgoing = lax.dynamic_index_in_dim(blocks, (pos + step) % size, 0, keepdims=False)
        total = total + shift_ring(outgoing, axis, size, step)
    return total


def local(
    patch_features_window,
    probe_request_heads,
    lookup_projection,
    content_projection,
    final_projection,
    prior_picture_entries,
    caption_features,
    partner_indices,
    score_scale_param,
    score_shift,
):
    row_count = caption_features.shape[0]
    prior_count = prior_picture_entries.shape[0]
    section_size = lax.axis_size("section")
    mp_size = lax.axis_size("mp")
    inner_size = section_size * mp_size
    section_pos = lax.axis_index("section")
    mp_pos = lax.axis_index("mp")
    inner_pos = section_pos * mp_size + mp_pos
    outer_pos = lax.axis_index(("x", "zh", "core"))
    x_size, zh_size, core_size = lax.axis_size("x"), lax.axis_size("zh"), lax.axis_size("core")
    outer_size = x_size * zh_size * core_size
    score_scaling = score_scale_param[0]
    starting_position = score_shift[0]

    text_unit, text_inverse = normalize_rows(caption_features)
    caption_magnitude = text_unit.astype(jnp.bfloat16)
    device_portion_count = lax.all_gather(caption_magnitude, ("x", "zh", "core"), axis=0, tiled=True)

    chunk_rows = row_count
    prior_norm = normalize_rows(
        jnp.pad(prior_picture_entries, ((0, chunk_rows - prior_count), (0, 0)))
    )[0].astype(jnp.bfloat16)
    prior_tile, device_portion_count = ring_gather(
        ring_gather(prior_norm, "mp", mp_size),
        "section",
        section_size,
        held=device_portion_count,
        held_step=section_size // 2,
    )

    pooled = pool_image(
        patch_features_window[0],
        probe_request_heads,
        lookup_projection,
        content_projection,
        final_projection,
    )
    pooled_norm = normalize_rows(pooled)[0].astype(jnp.bfloat16)
    pooled_tile = lax.all_to_all(
        jnp.broadcast_to(pooled_norm, (inner_size, pooled_norm.shape[1])),
        ("section", "mp"),
        0,
        0,
        tiled=True,
    )
    picture_tile = jnp.concatenate([prior_tile, pooled_tile], axis=0)

    group_labels = lax.dynamic_slice_in_dim(
        partner_indices, outer_pos * (inner_size * row_count), inner_size * row_count
    ).reshape(section_size, mp_size, row_count)
    ring_labels = jnp.roll(jnp.roll(group_labels, -section_pos, axis=0), -mp_pos, axis=1)
    prior_labels = jnp.concatenate(
        [
            ring_labels[:, :, 1 : 1 + prior_count],
            jnp.full((section_size, mp_size, chunk_rows - prior_count), -1, jnp.int32),
        ],
        axis=2,
    ).reshape(-1)
    pooled_labels = group_labels[:, :, 0].reshape(-1)
    target_tile = jnp.concatenate([prior_labels, pooled_labels])

    width = device_portion_count.shape[1]
    device_portion_count = (
        device_portion_count.reshape(x_size, zh_size, core_size, row_count, width)
        .transpose(2, 0, 1, 3, 4)
        .reshape(outer_size * row_count, width)
    )
    blocks = jnp.arange(outer_size, dtype=jnp.int32)
    block_core = blocks // (x_size * zh_size)
    block_x = blocks // zh_size % x_size
    block_zh = blocks % zh_size
    block_dp = block_x * (zh_size * core_size) + block_zh * core_size + block_core
    overall_column_indices = (
        (block_dp * inner_size + inner_pos)[:, None] * row_count
        + jnp.arange(row_count, dtype=jnp.int32)[None, :]
    ).reshape(-1)

    row_losses, grad_terms = block_contributions(
        picture_tile,
        target_tile,
        device_portion_count,
        overall_column_indices,
        score_scaling,
        starting_position,
    )
    prior_losses = row_losses[: inner_size * chunk_rows].reshape(section_size, mp_size, chunk_rows)
    prior_losses = jnp.roll(jnp.roll(prior_losses, section_pos, axis=0), mp_pos, axis=1)
    pooled_losses = row_losses[inner_size * chunk_rows :]
    loss_parts = jnp.concatenate(
        [pooled_losses[:, None], prior_losses.reshape(inner_size, chunk_rows)[:, :prior_count]],
        axis=1,
    )
    core_terms = direct_scatter(grad_terms, "core", core_size)
    loss_parts, core_terms = lax.optimization_barrier((loss_parts, core_terms))
    own_losses = jnp.sum(
        lax.all_to_all(loss_parts, ("section", "mp"), 0, 0, tiled=True), axis=0
    )
    x_terms = direct_scatter(core_terms, "x", x_size)
    own_losses, x_terms = lax.optimization_barrier((own_losses, x_terms))
    own_terms = direct_scatter(x_terms, "zh", zh_size)
    along = jnp.sum(text_unit * own_terms, axis=1, keepdims=True)
    text_grad = (own_terms - text_unit * along) * text_inverse
    return (own_losses, text_grad)


def solution(mesh):
    outer = mesh.shape["dp"]
    core_size = 2
    x_size = outer // (core_size * 3)
    fine_mesh = jax.sharding.Mesh(
        mesh.devices.reshape(x_size, 3, core_size, mesh.shape["section"], mesh.shape["mp"]),
        ("x", "zh", "core", "section", "mp"),
    )
    spread = ("x", "zh", "core", "section", "mp")
    placed = (
        P(spread, None, None),
        P(),
        P(),
        P(),
        P(),
        P(spread, None),
        P(spread, None),
        P(),
        P(),
        P(),
    )
    return jax.shard_map(
        local,
        mesh=fine_mesh,
        in_specs=placed,
        out_specs=(P(spread), P(spread, None)),
        check_vma=False,
    )
```

```python
import math

import jax
import jax.numpy as jnp
from jax import lax
from jax.sharding import PartitionSpec as P

HEADS = 16
HD = 72


def pool_image(
    patch_rows, probe_request_heads, lookup_projection, content_projection, final_projection
):
    width = lookup_projection.shape[0]
    head_of_column = jnp.arange(width, dtype=jnp.int32) // HD
    probe_blocks = jnp.where(
        head_of_column[:, None] == jnp.arange(HEADS, dtype=jnp.int32)[None, :],
        probe_request_heads[:, None],
        jnp.zeros((), probe_request_heads.dtype),
    )
    key_probe = jnp.dot(lookup_projection, probe_blocks, preferred_element_type=jnp.float32)
    key_probe = (key_probe / math.sqrt(HD)).astype(jnp.bfloat16)
    scores = jnp.dot(patch_rows, key_probe, preferred_element_type=jnp.float32)
    highest = jnp.max(scores, axis=0, keepdims=True)
    exponent = jnp.exp(scores - highest)
    weights = (exponent / jnp.sum(exponent, axis=0, keepdims=True)).astype(jnp.bfloat16)
    pooled_patch = lax.dot_general(
        weights, patch_rows, (((0,), (0,)), ((), ())), preferred_element_type=jnp.float32
    ).astype(jnp.bfloat16)
    every_head = jnp.dot(pooled_patch, content_projection, preferred_element_type=jnp.float32)
    values = jnp.sum(
        every_head.reshape(HEADS, HEADS, HD)
        * jnp.eye(HEADS, dtype=jnp.float32)[:, :, None],
        axis=1,
    )
    values = values.astype(jnp.bfloat16).reshape(1, width)
    return jnp.dot(values, final_projection, preferred_element_type=jnp.float32).astype(
        jnp.bfloat16
    )


def normalize_rows(rows_in):
    widened = rows_in.astype(jnp.float32)
    inverse = lax.rsqrt(jnp.sum(widened * widened, axis=1, keepdims=True) + 1e-06)
    return (widened * inverse, inverse)


def block_contributions(
    picture_tile,
    target_tile,
    device_portion_count,
    overall_column_indices,
    score_scaling,
    starting_position,
):
    pair_scores = (
        score_scaling
        * lax.dot_general(
            picture_tile,
            device_portion_count,
            (((1,), (1,)), ((), ())),
            preferred_element_type=jnp.float32,
        )
        + starting_position
    )
    matching_flag = target_tile[:, None] == overall_column_indices[None, :]
    row_losses = jnp.sum(
        jax.nn.softplus(jnp.where(matching_flag, -pair_scores, pair_scores)), axis=1
    )
    sigmoid_derivatives = (
        (jax.nn.sigmoid(pair_scores) - matching_flag.astype(jnp.float32)) * score_scaling
    ).astype(jnp.bfloat16)
    return (row_losses, sigmoid_derivatives)


def column_terms(sigmoid_derivatives, picture_tile, start, count):
    return lax.dot_general(
        lax.dynamic_slice_in_dim(sigmoid_derivatives, start, count, axis=1),
        picture_tile,
        (((0,), (0,)), ((), ())),
        preferred_element_type=jnp.float32,
    )


def shift_ring(x, axis, size, step):
    return lax.ppermute(x, axis, [(i, (i + step) % size) for i in range(size)])


def ring_gather(x, axis, size, held=None, held_step=0):
    forward, backward = x, x
    arrived = {0: x}
    forward_steps = size // 2
    backward_steps = size - 1 - forward_steps
    for step in range(1, forward_steps + 1):
        if held is not None and step == held_step:
            forward, held = lax.optimization_barrier((forward, held))
        forward = shift_ring(forward, axis, size, 1)
        arrived[(size - step) % size] = forward
        if step <= backward_steps:
            backward = shift_ring(backward, axis, size, -1)
            arrived[step] = backward
    tile = jnp.concatenate([arrived[d] for d in range(size)], axis=0)
    return tile if held is None else (tile, held)


def direct_gather(x, axis, size):
    return jnp.concatenate(
        [x] + [shift_ring(x, axis, size, -step) for step in range(1, size)], axis=0
    )


def direct_scatter(x, axis, size):
    pos = lax.axis_index(axis)
    blocks = x.reshape(size, x.shape[0] // size, *x.shape[1:])
    total = lax.dynamic_index_in_dim(blocks, pos, 0, keepdims=False)
    for step in range(1, size):
        outgoing = lax.dynamic_index_in_dim(blocks, (pos + step) % size, 0, keepdims=False)
        total = total + shift_ring(outgoing, axis, size, step)
    return total


def local(
    patch_features_window,
    probe_request_heads,
    lookup_projection,
    content_projection,
    final_projection,
    prior_picture_entries,
    caption_features,
    partner_indices,
    score_scale_param,
    score_shift,
):
    row_count = caption_features.shape[0]
    prior_count = prior_picture_entries.shape[0]
    section_size = lax.axis_size("section")
    mp_size = lax.axis_size("mp")
    inner_size = section_size * mp_size
    section_pos = lax.axis_index("section")
    mp_pos = lax.axis_index("mp")
    inner_pos = section_pos * mp_size + mp_pos
    outer_pos = lax.axis_index(("x", "zh", "core"))
    x_size, zh_size, core_size = lax.axis_size("x"), lax.axis_size("zh"), lax.axis_size("core")
    outer_size = x_size * zh_size * core_size
    score_scaling = score_scale_param[0]
    starting_position = score_shift[0]

    text_unit, text_inverse = normalize_rows(caption_features)
    caption_magnitude = text_unit.astype(jnp.bfloat16)
    device_portion_count = lax.all_gather(caption_magnitude, ("x", "zh", "core"), axis=0, tiled=True)

    chunk_rows = row_count
    prior_norm = normalize_rows(
        jnp.pad(prior_picture_entries, ((0, chunk_rows - prior_count), (0, 0)))
    )[0].astype(jnp.bfloat16)
    prior_tile, device_portion_count = ring_gather(
        direct_gather(prior_norm, "mp", mp_size),
        "section",
        section_size,
        held=device_portion_count,
        held_step=section_size // 2,
    )

    pooled = pool_image(
        patch_features_window[0],
        probe_request_heads,
        lookup_projection,
        content_projection,
        final_projection,
    )
    pooled_norm = normalize_rows(pooled)[0].astype(jnp.bfloat16)
    pooled_tile = lax.all_to_all(
        jnp.broadcast_to(pooled_norm, (inner_size, pooled_norm.shape[1])),
        ("section", "mp"),
        0,
        0,
        tiled=True,
    )
    picture_tile = jnp.concatenate([prior_tile, pooled_tile], axis=0)

    group_labels = lax.dynamic_slice_in_dim(
        partner_indices, outer_pos * (inner_size * row_count), inner_size * row_count
    ).reshape(section_size, mp_size, row_count)
    ring_labels = jnp.roll(jnp.roll(group_labels, -section_pos, axis=0), -mp_pos, axis=1)
    prior_labels = jnp.concatenate(
        [
            ring_labels[:, :, 1 : 1 + prior_count],
            jnp.full((section_size, mp_size, chunk_rows - prior_count), -1, jnp.int32),
        ],
        axis=2,
    ).reshape(-1)
    pooled_labels = group_labels[:, :, 0].reshape(-1)
    target_tile = jnp.concatenate([prior_labels, pooled_labels])

    width = device_portion_count.shape[1]
    device_portion_count = (
        device_portion_count.reshape(x_size, zh_size, core_size, row_count, width)
        .transpose(2, 0, 1, 3, 4)
        .reshape(outer_size * row_count, width)
    )
    blocks = jnp.arange(outer_size, dtype=jnp.int32)
    block_core = blocks // (x_size * zh_size)
    block_x = blocks // zh_size % x_size
    block_zh = blocks % zh_size
    block_dp = block_x * (zh_size * core_size) + block_zh * core_size + block_core
    overall_column_indices = (
        (block_dp * inner_size + inner_pos)[:, None] * row_count
        + jnp.arange(row_count, dtype=jnp.int32)[None, :]
    ).reshape(-1)

    row_losses, sigmoid_derivatives = block_contributions(
        picture_tile,
        target_tile,
        device_portion_count,
        overall_column_indices,
        score_scaling,
        starting_position,
    )
    prior_losses = row_losses[: inner_size * chunk_rows].reshape(section_size, mp_size, chunk_rows)
    prior_losses = jnp.roll(jnp.roll(prior_losses, section_pos, axis=0), mp_pos, axis=1)
    pooled_losses = row_losses[inner_size * chunk_rows :]
    loss_parts = jnp.concatenate(
        [pooled_losses[:, None], prior_losses.reshape(inner_size, chunk_rows)[:, :prior_count]],
        axis=1,
    )
    core_pos = lax.axis_index("core")
    core_cols = device_portion_count.shape[0] // core_size
    core_terms = column_terms(sigmoid_derivatives, picture_tile, core_pos * core_cols, core_cols)
    for step in range(1, core_size):
        outgoing = column_terms(
            sigmoid_derivatives, picture_tile, (core_pos + step) % core_size * core_cols, core_cols
        )
        core_terms = core_terms + shift_ring(outgoing, "core", core_size, step)
    loss_parts, core_terms = lax.optimization_barrier((loss_parts, core_terms))
    own_losses = jnp.sum(
        lax.all_to_all(loss_parts, ("section", "mp"), 0, 0, tiled=True), axis=0
    )
    x_terms = direct_scatter(core_terms, "x", x_size)
    own_losses, x_terms = lax.optimization_barrier((own_losses, x_terms))
    own_terms = direct_scatter(x_terms, "zh", zh_size)
    along = jnp.sum(text_unit * own_terms, axis=1, keepdims=True)
    text_grad = (own_terms - text_unit * along) * text_inverse
    return (own_losses, text_grad)


def solution(mesh):
    outer = mesh.shape["dp"]
    core_size = 2
    x_size = outer // (core_size * 3)
    fine_mesh = jax.sharding.Mesh(
        mesh.devices.reshape(x_size, 3, core_size, mesh.shape["section"], mesh.shape["mp"]),
        ("x", "zh", "core", "section", "mp"),
    )
    spread = ("x", "zh", "core", "section", "mp")
    placed = (
        P(spread, None, None),
        P(),
        P(),
        P(),
        P(),
        P(spread, None),
        P(spread, None),
        P(),
        P(),
        P(),
    )
    return jax.shard_map(
        local,
        mesh=fine_mesh,
        in_specs=placed,
        out_specs=(P(spread), P(spread, None)),
        check_vma=False,
    )
```

```python
import math

import jax
import jax.numpy as jnp
from jax import lax
from jax.sharding import PartitionSpec as P

HEADS = 16
HD = 72


def pool_image(
    patch_rows, probe_request_heads, lookup_projection, content_projection, final_projection
):
    width = lookup_projection.shape[0]
    head_of_column = jnp.arange(width, dtype=jnp.int32) // HD
    probe_blocks = jnp.where(
        head_of_column[:, None] == jnp.arange(HEADS, dtype=jnp.int32)[None, :],
        probe_request_heads[:, None],
        jnp.zeros((), probe_request_heads.dtype),
    )
    key_probe = jnp.dot(lookup_projection, probe_blocks, preferred_element_type=jnp.float32)
    key_probe = (key_probe / math.sqrt(HD)).astype(jnp.bfloat16)
    scores = jnp.dot(patch_rows, key_probe, preferred_element_type=jnp.float32)
    highest = jnp.max(scores, axis=0, keepdims=True)
    exponent = jnp.exp(scores - highest)
    weights = (exponent / jnp.sum(exponent, axis=0, keepdims=True)).astype(jnp.bfloat16)
    pooled_patch = lax.dot_general(
        weights, patch_rows, (((0,), (0,)), ((), ())), preferred_element_type=jnp.float32
    ).astype(jnp.bfloat16)
    every_head = jnp.dot(pooled_patch, content_projection, preferred_element_type=jnp.float32)
    values = jnp.sum(
        every_head.reshape(HEADS, HEADS, HD)
        * jnp.eye(HEADS, dtype=jnp.float32)[:, :, None],
        axis=1,
    )
    values = values.astype(jnp.bfloat16).reshape(1, width)
    return jnp.dot(values, final_projection, preferred_element_type=jnp.float32).astype(
        jnp.bfloat16
    )


def normalize_rows(rows_in):
    widened = rows_in.astype(jnp.float32)
    inverse = lax.rsqrt(jnp.sum(widened * widened, axis=1, keepdims=True) + 1e-06)
    return (widened * inverse, inverse)


def block_contributions(
    picture_tile,
    target_tile,
    device_portion_count,
    overall_column_indices,
    score_scaling,
    starting_position,
):
    pair_scores = (
        score_scaling
        * lax.dot_general(
            picture_tile,
            device_portion_count,
            (((1,), (1,)), ((), ())),
            preferred_element_type=jnp.float32,
        )
        + starting_position
    )
    matching_flag = target_tile[:, None] == overall_column_indices[None, :]
    row_losses = jnp.sum(
        jax.nn.softplus(jnp.where(matching_flag, -pair_scores, pair_scores)), axis=1
    )
    sigmoid_derivatives = (
        (jax.nn.sigmoid(pair_scores) - matching_flag.astype(jnp.float32)) * score_scaling
    ).astype(jnp.bfloat16)
    grad_terms = lax.dot_general(
        sigmoid_derivatives,
        picture_tile,
        (((0,), (0,)), ((), ())),
        preferred_element_type=jnp.float32,
    )
    return (row_losses, grad_terms)


def shift_ring(x, axis, size, step):
    return lax.ppermute(x, axis, [(i, (i + step) % size) for i in range(size)])


def ring_gather(x, axis, size, held=None, held_step=0):
    forward, backward = x, x
    arrived = {0: x}
    forward_steps = size // 2
    backward_steps = size - 1 - forward_steps
    for step in range(1, forward_steps + 1):
        if held is not None and step == held_step:
            forward, held = lax.optimization_barrier((forward, held))
        forward = shift_ring(forward, axis, size, 1)
        arrived[(size - step) % size] = forward
        if step <= backward_steps:
            backward = shift_ring(backward, axis, size, -1)
            arrived[step] = backward
    tile = jnp.concatenate([arrived[d] for d in range(size)], axis=0)
    return tile if held is None else (tile, held)


def direct_scatter(x, axis, size):
    pos = lax.axis_index(axis)
    blocks = x.reshape(size, x.shape[0] // size, *x.shape[1:])
    total = lax.dynamic_index_in_dim(blocks, pos, 0, keepdims=False)
    for step in range(1, size):
        outgoing = lax.dynamic_index_in_dim(blocks, (pos + step) % size, 0, keepdims=False)
        total = total + shift_ring(outgoing, axis, size, step)
    return total


def local(
    patch_features_window,
    probe_request_heads,
    lookup_projection,
    content_projection,
    final_projection,
    prior_picture_entries,
    caption_features,
    partner_indices,
    score_scale_param,
    score_shift,
):
    row_count = caption_features.shape[0]
    prior_count = prior_picture_entries.shape[0]
    section_size = lax.axis_size("section")
    mp_size = lax.axis_size("mp")
    inner_size = section_size * mp_size
    section_pos = lax.axis_index("section")
    mp_pos = lax.axis_index("mp")
    inner_pos = section_pos * mp_size + mp_pos
    outer_pos = lax.axis_index(("x", "zh", "core"))
    x_size, zh_size, core_size = lax.axis_size("x"), lax.axis_size("zh"), lax.axis_size("core")
    outer_size = x_size * zh_size * core_size
    score_scaling = score_scale_param[0]
    starting_position = score_shift[0]

    text_unit, text_inverse = normalize_rows(caption_features)
    caption_magnitude = text_unit.astype(jnp.bfloat16)
    device_portion_count = lax.all_gather(caption_magnitude, ("x", "zh", "core"), axis=0, tiled=True)

    chunk_rows = row_count
    prior_norm = normalize_rows(
        jnp.pad(prior_picture_entries, ((0, chunk_rows - prior_count), (0, 0)))
    )[0].astype(jnp.bfloat16)
    prior_tile, device_portion_count = ring_gather(
        ring_gather(prior_norm, "mp", mp_size),
        "section",
        section_size,
        held=device_portion_count,
        held_step=section_size // 2,
    )

    pooled = pool_image(
        patch_features_window[0],
        probe_request_heads,
        lookup_projection,
        content_projection,
        final_projection,
    )
    pooled_norm = normalize_rows(pooled)[0].astype(jnp.bfloat16)
    pooled_tile = lax.all_to_all(
        jnp.broadcast_to(pooled_norm, (inner_size, pooled_norm.shape[1])),
        ("section", "mp"),
        0,
        0,
        tiled=True,
    )
    picture_tile = jnp.concatenate([prior_tile, pooled_tile], axis=0)

    group_labels = lax.dynamic_slice_in_dim(
        partner_indices, outer_pos * (inner_size * row_count), inner_size * row_count
    ).reshape(section_size, mp_size, row_count)
    ring_labels = jnp.roll(jnp.roll(group_labels, -section_pos, axis=0), -mp_pos, axis=1)
    prior_labels = jnp.concatenate(
        [
            ring_labels[:, :, 1 : 1 + prior_count],
            jnp.full((section_size, mp_size, chunk_rows - prior_count), -1, jnp.int32),
        ],
        axis=2,
    ).reshape(-1)
    pooled_labels = group_labels[:, :, 0].reshape(-1)
    target_tile = jnp.concatenate([prior_labels, pooled_labels])

    width = device_portion_count.shape[1]
    device_portion_count = (
        device_portion_count.reshape(x_size, zh_size, core_size, row_count, width)
        .transpose(2, 0, 1, 3, 4)
        .reshape(outer_size * row_count, width)
    )
    blocks = jnp.arange(outer_size, dtype=jnp.int32)
    block_core = blocks // (x_size * zh_size)
    block_x = blocks // zh_size % x_size
    block_zh = blocks % zh_size
    block_dp = block_x * (zh_size * core_size) + block_zh * core_size + block_core
    overall_column_indices = (
        (block_dp * inner_size + inner_pos)[:, None] * row_count
        + jnp.arange(row_count, dtype=jnp.int32)[None, :]
    ).reshape(-1)

    row_losses, grad_terms = block_contributions(
        picture_tile,
        target_tile,
        device_portion_count,
        overall_column_indices,
        score_scaling,
        starting_position,
    )
    prior_losses = row_losses[: inner_size * chunk_rows].reshape(section_size, mp_size, chunk_rows)
    prior_losses = jnp.roll(jnp.roll(prior_losses, section_pos, axis=0), mp_pos, axis=1)
    pooled_losses = row_losses[inner_size * chunk_rows :]
    loss_parts = jnp.concatenate(
        [pooled_losses[:, None], prior_losses.reshape(inner_size, chunk_rows)[:, :prior_count]],
        axis=1,
    )
    core_terms = direct_scatter(grad_terms, "core", core_size)
    loss_parts, core_terms = lax.optimization_barrier((loss_parts, core_terms))
    section_losses = jnp.sum(
        lax.all_to_all(
            loss_parts.reshape(section_size, mp_size, row_count), "mp", 1, 1, tiled=True
        ),
        axis=1,
    )
    x_terms = direct_scatter(core_terms, "x", x_size)
    section_losses, x_terms = lax.optimization_barrier((section_losses, x_terms))
    own_losses = jnp.sum(lax.all_to_all(section_losses, "section", 0, 0, tiled=True), axis=0)
    own_terms = direct_scatter(x_terms, "zh", zh_size)
    along = jnp.sum(text_unit * own_terms, axis=1, keepdims=True)
    text_grad = (own_terms - text_unit * along) * text_inverse
    return (own_losses, text_grad)


def solution(mesh):
    outer = mesh.shape["dp"]
    core_size = 2
    x_size = outer // (core_size * 3)
    fine_mesh = jax.sharding.Mesh(
        mesh.devices.reshape(x_size, 3, core_size, mesh.shape["section"], mesh.shape["mp"]),
        ("x", "zh", "core", "section", "mp"),
    )
    spread = ("x", "zh", "core", "section", "mp")
    placed = (
        P(spread, None, None),
        P(),
        P(),
        P(),
        P(),
        P(spread, None),
        P(spread, None),
        P(),
        P(),
        P(),
    )
    return jax.shard_map(
        local,
        mesh=fine_mesh,
        in_specs=placed,
        out_specs=(P(spread), P(spread, None)),
        check_vma=False,
    )
```

```python
import math

import jax
import jax.numpy as jnp
from jax import lax
from jax.sharding import PartitionSpec as P

HEADS = 16
HD = 72


def pool_image(
    patch_rows, probe_request_heads, lookup_projection, content_projection, final_projection
):
    width = lookup_projection.shape[0]
    head_of_column = jnp.arange(width, dtype=jnp.int32) // HD
    probe_blocks = jnp.where(
        head_of_column[:, None] == jnp.arange(HEADS, dtype=jnp.int32)[None, :],
        probe_request_heads[:, None],
        jnp.zeros((), probe_request_heads.dtype),
    )
    key_probe = jnp.dot(lookup_projection, probe_blocks, preferred_element_type=jnp.float32)
    key_probe = (key_probe / math.sqrt(HD)).astype(jnp.bfloat16)
    scores = jnp.dot(patch_rows, key_probe, preferred_element_type=jnp.float32)
    highest = jnp.max(scores, axis=0, keepdims=True)
    exponent = jnp.exp(scores - highest)
    weights = (exponent / jnp.sum(exponent, axis=0, keepdims=True)).astype(jnp.bfloat16)
    pooled_patch = lax.dot_general(
        weights, patch_rows, (((0,), (0,)), ((), ())), preferred_element_type=jnp.float32
    ).astype(jnp.bfloat16)
    every_head = jnp.dot(pooled_patch, content_projection, preferred_element_type=jnp.float32)
    values = jnp.sum(
        every_head.reshape(HEADS, HEADS, HD)
        * jnp.eye(HEADS, dtype=jnp.float32)[:, :, None],
        axis=1,
    )
    values = values.astype(jnp.bfloat16).reshape(1, width)
    return jnp.dot(values, final_projection, preferred_element_type=jnp.float32).astype(
        jnp.bfloat16
    )


def normalize_rows(rows_in):
    widened = rows_in.astype(jnp.float32)
    inverse = lax.rsqrt(jnp.sum(widened * widened, axis=1, keepdims=True) + 1e-06)
    return (widened * inverse, inverse)


def block_contributions(
    picture_tile,
    target_tile,
    device_portion_count,
    overall_column_indices,
    score_scaling,
    starting_position,
):
    pair_scores = (
        score_scaling
        * lax.dot_general(
            picture_tile,
            device_portion_count,
            (((1,), (1,)), ((), ())),
            preferred_element_type=jnp.float32,
        )
        + starting_position
    )
    matching_flag = target_tile[:, None] == overall_column_indices[None, :]
    row_losses = jnp.sum(
        jax.nn.softplus(jnp.where(matching_flag, -pair_scores, pair_scores)), axis=1
    )
    sigmoid_derivatives = (
        (jax.nn.sigmoid(pair_scores) - matching_flag.astype(jnp.float32)) * score_scaling
    ).astype(jnp.bfloat16)
    grad_terms = lax.dot_general(
        sigmoid_derivatives,
        picture_tile,
        (((0,), (0,)), ((), ())),
        preferred_element_type=jnp.float32,
    )
    return (row_losses, grad_terms)


def shift_ring(x, axis, size, step):
    return lax.ppermute(x, axis, [(i, (i + step) % size) for i in range(size)])


def ring_gather(x, axis, size, held=None, held_step=0):
    forward, backward = x, x
    arrived = {0: x}
    forward_steps = size // 2
    backward_steps = size - 1 - forward_steps
    for step in range(1, forward_steps + 1):
        if held is not None and step == held_step:
            forward, held = lax.optimization_barrier((forward, held))
        forward = shift_ring(forward, axis, size, 1)
        arrived[(size - step) % size] = forward
        if step <= backward_steps:
            backward = shift_ring(backward, axis, size, -1)
            arrived[step] = backward
    tile = jnp.concatenate([arrived[d] for d in range(size)], axis=0)
    return tile if held is None else (tile, held)


def direct_scatter(x, axis, size):
    pos = lax.axis_index(axis)
    blocks = x.reshape(size, x.shape[0] // size, *x.shape[1:])
    total = lax.dynamic_index_in_dim(blocks, pos, 0, keepdims=False)
    for step in range(1, size):
        outgoing = lax.dynamic_index_in_dim(blocks, (pos + step) % size, 0, keepdims=False)
        total = total + shift_ring(outgoing, axis, size, step)
    return total


def local(
    patch_features_window,
    probe_request_heads,
    lookup_projection,
    content_projection,
    final_projection,
    prior_picture_entries,
    caption_features,
    partner_indices,
    score_scale_param,
    score_shift,
):
    row_count = caption_features.shape[0]
    prior_count = prior_picture_entries.shape[0]
    section_size = lax.axis_size("section")
    mp_size = lax.axis_size("mp")
    inner_size = section_size * mp_size
    section_pos = lax.axis_index("section")
    mp_pos = lax.axis_index("mp")
    inner_pos = section_pos * mp_size + mp_pos
    outer_pos = lax.axis_index(("x", "zh", "core"))
    x_size, zh_size, core_size = lax.axis_size("x"), lax.axis_size("zh"), lax.axis_size("core")
    outer_size = x_size * zh_size * core_size
    score_scaling = score_scale_param[0]
    starting_position = score_shift[0]

    text_unit, text_inverse = normalize_rows(caption_features)
    device_portion_count = lax.all_gather(caption_features, ("x", "zh", "core"), axis=0, tiled=True)

    chunk_rows = row_count
    prior_norm = normalize_rows(
        jnp.pad(prior_picture_entries, ((0, chunk_rows - prior_count), (0, 0)))
    )[0].astype(jnp.bfloat16)
    prior_tile, device_portion_count = ring_gather(
        ring_gather(prior_norm, "mp", mp_size),
        "section",
        section_size,
        held=device_portion_count,
        held_step=section_size // 2,
    )

    pooled = pool_image(
        patch_features_window[0],
        probe_request_heads,
        lookup_projection,
        content_projection,
        final_projection,
    )
    pooled_norm = normalize_rows(pooled)[0].astype(jnp.bfloat16)
    pooled_tile = lax.all_to_all(
        jnp.broadcast_to(pooled_norm, (inner_size, pooled_norm.shape[1])),
        ("section", "mp"),
        0,
        0,
        tiled=True,
    )
    picture_tile = jnp.concatenate([prior_tile, pooled_tile], axis=0)

    group_labels = lax.dynamic_slice_in_dim(
        partner_indices, outer_pos * (inner_size * row_count), inner_size * row_count
    ).reshape(section_size, mp_size, row_count)
    ring_labels = jnp.roll(jnp.roll(group_labels, -section_pos, axis=0), -mp_pos, axis=1)
    prior_labels = jnp.concatenate(
        [
            ring_labels[:, :, 1 : 1 + prior_count],
            jnp.full((section_size, mp_size, chunk_rows - prior_count), -1, jnp.int32),
        ],
        axis=2,
    ).reshape(-1)
    pooled_labels = group_labels[:, :, 0].reshape(-1)
    target_tile = jnp.concatenate([prior_labels, pooled_labels])

    width = device_portion_count.shape[1]
    device_portion_count = (
        device_portion_count.reshape(x_size, zh_size, core_size, row_count, width)
        .transpose(2, 0, 1, 3, 4)
        .reshape(outer_size * row_count, width)
    )
    blocks = jnp.arange(outer_size, dtype=jnp.int32)
    block_core = blocks // (x_size * zh_size)
    block_x = blocks // zh_size % x_size
    block_zh = blocks % zh_size
    block_dp = block_x * (zh_size * core_size) + block_zh * core_size + block_core
    overall_column_indices = (
        (block_dp * inner_size + inner_pos)[:, None] * row_count
        + jnp.arange(row_count, dtype=jnp.int32)[None, :]
    ).reshape(-1)

    device_portion_count = normalize_rows(device_portion_count)[0].astype(jnp.bfloat16)
    row_losses, grad_terms = block_contributions(
        picture_tile,
        target_tile,
        device_portion_count,
        overall_column_indices,
        score_scaling,
        starting_position,
    )
    prior_losses = row_losses[: inner_size * chunk_rows].reshape(section_size, mp_size, chunk_rows)
    prior_losses = jnp.roll(jnp.roll(prior_losses, section_pos, axis=0), mp_pos, axis=1)
    pooled_losses = row_losses[inner_size * chunk_rows :]
    loss_parts = jnp.concatenate(
        [pooled_losses[:, None], prior_losses.reshape(inner_size, chunk_rows)[:, :prior_count]],
        axis=1,
    )
    core_terms = direct_scatter(grad_terms, "core", core_size)
    loss_parts, core_terms = lax.optimization_barrier((loss_parts, core_terms))
    section_losses = jnp.sum(
        lax.all_to_all(
            loss_parts.reshape(section_size, mp_size, row_count), "mp", 1, 1, tiled=True
        ),
        axis=1,
    )
    x_terms = direct_scatter(core_terms, "x", x_size)
    section_losses, x_terms = lax.optimization_barrier((section_losses, x_terms))
    own_losses = jnp.sum(lax.all_to_all(section_losses, "section", 0, 0, tiled=True), axis=0)
    own_terms = direct_scatter(x_terms, "zh", zh_size)
    along = jnp.sum(text_unit * own_terms, axis=1, keepdims=True)
    text_grad = (own_terms - text_unit * along) * text_inverse
    return (own_losses, text_grad)


def solution(mesh):
    outer = mesh.shape["dp"]
    core_size = 2
    x_size = outer // (core_size * 3)
    fine_mesh = jax.sharding.Mesh(
        mesh.devices.reshape(x_size, 3, core_size, mesh.shape["section"], mesh.shape["mp"]),
        ("x", "zh", "core", "section", "mp"),
    )
    spread = ("x", "zh", "core", "section", "mp")
    placed = (
        P(spread, None, None),
        P(),
        P(),
        P(),
        P(),
        P(spread, None),
        P(spread, None),
        P(),
        P(),
        P(),
    )
    return jax.shard_map(
        local,
        mesh=fine_mesh,
        in_specs=placed,
        out_specs=(P(spread), P(spread, None)),
        check_vma=False,
    )
```

```python
import math

import jax
import jax.numpy as jnp
from jax import lax
from jax.sharding import PartitionSpec as P

HEADS = 16
HD = 72


def pool_image(
    patch_rows, probe_request_heads, lookup_projection, content_projection, final_projection
):
    width = lookup_projection.shape[0]
    head_of_column = jnp.arange(width, dtype=jnp.int32) // HD
    probe_blocks = jnp.where(
        head_of_column[:, None] == jnp.arange(HEADS, dtype=jnp.int32)[None, :],
        probe_request_heads[:, None],
        jnp.zeros((), probe_request_heads.dtype),
    )
    key_probe = jnp.dot(lookup_projection, probe_blocks, preferred_element_type=jnp.float32)
    key_probe = (key_probe / math.sqrt(HD)).astype(jnp.bfloat16)
    scores = jnp.dot(patch_rows, key_probe, preferred_element_type=jnp.float32)
    highest = jnp.max(scores, axis=0, keepdims=True)
    exponent = jnp.exp(scores - highest)
    weights = (exponent / jnp.sum(exponent, axis=0, keepdims=True)).astype(jnp.bfloat16)
    pooled_patch = lax.dot_general(
        weights, patch_rows, (((0,), (0,)), ((), ())), preferred_element_type=jnp.float32
    ).astype(jnp.bfloat16)
    every_head = jnp.dot(pooled_patch, content_projection, preferred_element_type=jnp.float32)
    values = jnp.sum(
        every_head.reshape(HEADS, HEADS, HD)
        * jnp.eye(HEADS, dtype=jnp.float32)[:, :, None],
        axis=1,
    )
    values = values.astype(jnp.bfloat16).reshape(1, width)
    return jnp.dot(values, final_projection, preferred_element_type=jnp.float32).astype(
        jnp.bfloat16
    )


def normalize_rows(rows_in):
    widened = rows_in.astype(jnp.float32)
    inverse = lax.rsqrt(jnp.sum(widened * widened, axis=1, keepdims=True) + 1e-06)
    return (widened * inverse, inverse)


def block_contributions(
    picture_tile,
    target_tile,
    device_portion_count,
    overall_column_indices,
    score_scaling,
    starting_position,
):
    pair_scores = (
        score_scaling
        * lax.dot_general(
            picture_tile,
            device_portion_count,
            (((1,), (1,)), ((), ())),
            preferred_element_type=jnp.float32,
        )
        + starting_position
    )
    matching_flag = target_tile[:, None] == overall_column_indices[None, :]
    row_losses = jnp.sum(
        jax.nn.softplus(jnp.where(matching_flag, -pair_scores, pair_scores)), axis=1
    )
    sigmoid_derivatives = (
        (jax.nn.sigmoid(pair_scores) - matching_flag.astype(jnp.float32)) * score_scaling
    ).astype(jnp.bfloat16)
    grad_terms = lax.dot_general(
        sigmoid_derivatives,
        picture_tile,
        (((0,), (0,)), ((), ())),
        preferred_element_type=jnp.float32,
    )
    return (row_losses, grad_terms)


def shift_ring(x, axis, size, step):
    return lax.ppermute(x, axis, [(i, (i + step) % size) for i in range(size)])


def ring_gather(x, axis, size, held=None, held_step=0):
    forward, backward = x, x
    arrived = {0: x}
    forward_steps = size // 2
    backward_steps = size - 1 - forward_steps
    for step in range(1, forward_steps + 1):
        if held is not None and step == held_step:
            forward, held = lax.optimization_barrier((forward, held))
        forward = shift_ring(forward, axis, size, 1)
        arrived[(size - step) % size] = forward
        if step <= backward_steps:
            backward = shift_ring(backward, axis, size, -1)
            arrived[step] = backward
    tile = jnp.concatenate([arrived[d] for d in range(size)], axis=0)
    return tile if held is None else (tile, held)


def direct_scatter(x, axis, size):
    pos = lax.axis_index(axis)
    blocks = x.reshape(size, x.shape[0] // size, *x.shape[1:])
    total = lax.dynamic_index_in_dim(blocks, pos, 0, keepdims=False)
    for step in range(1, size):
        outgoing = lax.dynamic_index_in_dim(blocks, (pos + step) % size, 0, keepdims=False)
        total = total + shift_ring(outgoing, axis, size, step)
    return total


def local(
    patch_features_window,
    probe_request_heads,
    lookup_projection,
    content_projection,
    final_projection,
    prior_picture_entries,
    caption_features,
    partner_indices,
    score_scale_param,
    score_shift,
):
    row_count = caption_features.shape[0]
    prior_count = prior_picture_entries.shape[0]
    section_size = lax.axis_size("section")
    mp_size = lax.axis_size("mp")
    inner_size = section_size * mp_size
    section_pos = lax.axis_index("section")
    mp_pos = lax.axis_index("mp")
    inner_pos = section_pos * mp_size + mp_pos
    outer_pos = lax.axis_index(("x", "zh", "core"))
    x_size, zh_size, core_size = lax.axis_size("x"), lax.axis_size("zh"), lax.axis_size("core")
    outer_size = x_size * zh_size * core_size
    score_scaling = score_scale_param[0]
    starting_position = score_shift[0]

    text_unit, text_inverse = normalize_rows(caption_features)
    caption_magnitude = text_unit.astype(jnp.bfloat16)
    device_portion_count = lax.all_gather(caption_magnitude, ("core", "x", "zh"), axis=0, tiled=True)

    chunk_rows = row_count
    prior_norm = normalize_rows(
        jnp.pad(prior_picture_entries, ((0, chunk_rows - prior_count), (0, 0)))
    )[0].astype(jnp.bfloat16)
    prior_tile, device_portion_count = ring_gather(
        ring_gather(prior_norm, "mp", mp_size),
        "section",
        section_size,
        held=device_portion_count,
        held_step=section_size // 2,
    )

    pooled = pool_image(
        patch_features_window[0],
        probe_request_heads,
        lookup_projection,
        content_projection,
        final_projection,
    )
    pooled_norm = normalize_rows(pooled)[0].astype(jnp.bfloat16)
    pooled_tile = lax.all_to_all(
        jnp.broadcast_to(pooled_norm, (inner_size, pooled_norm.shape[1])),
        ("section", "mp"),
        0,
        0,
        tiled=True,
    )
    picture_tile = jnp.concatenate([prior_tile, pooled_tile], axis=0)

    group_labels = lax.dynamic_slice_in_dim(
        partner_indices, outer_pos * (inner_size * row_count), inner_size * row_count
    ).reshape(section_size, mp_size, row_count)
    ring_labels = jnp.roll(jnp.roll(group_labels, -section_pos, axis=0), -mp_pos, axis=1)
    prior_labels = jnp.concatenate(
        [
            ring_labels[:, :, 1 : 1 + prior_count],
            jnp.full((section_size, mp_size, chunk_rows - prior_count), -1, jnp.int32),
        ],
        axis=2,
    ).reshape(-1)
    pooled_labels = group_labels[:, :, 0].reshape(-1)
    target_tile = jnp.concatenate([prior_labels, pooled_labels])

    blocks = jnp.arange(outer_size, dtype=jnp.int32)
    block_core = blocks // (x_size * zh_size)
    block_x = blocks // zh_size % x_size
    block_zh = blocks % zh_size
    block_dp = block_x * (zh_size * core_size) + block_zh * core_size + block_core
    overall_column_indices = (
        (block_dp * inner_size + inner_pos)[:, None] * row_count
        + jnp.arange(row_count, dtype=jnp.int32)[None, :]
    ).reshape(-1)

    row_losses, grad_terms = block_contributions(
        picture_tile,
        target_tile,
        device_portion_count,
        overall_column_indices,
        score_scaling,
        starting_position,
    )
    prior_losses = row_losses[: inner_size * chunk_rows].reshape(section_size, mp_size, chunk_rows)
    prior_losses = jnp.roll(jnp.roll(prior_losses, section_pos, axis=0), mp_pos, axis=1)
    pooled_losses = row_losses[inner_size * chunk_rows :]
    loss_parts = jnp.concatenate(
        [pooled_losses[:, None], prior_losses.reshape(inner_size, chunk_rows)[:, :prior_count]],
        axis=1,
    )
    core_terms = direct_scatter(grad_terms, "core", core_size)
    loss_parts, core_terms = lax.optimization_barrier((loss_parts, core_terms))
    section_losses = jnp.sum(
        lax.all_to_all(
            loss_parts.reshape(section_size, mp_size, row_count), "mp", 1, 1, tiled=True
        ),
        axis=1,
    )
    x_terms = direct_scatter(core_terms, "x", x_size)
    section_losses, x_terms = lax.optimization_barrier((section_losses, x_terms))
    own_losses = jnp.sum(lax.all_to_all(section_losses, "section", 0, 0, tiled=True), axis=0)
    own_terms = direct_scatter(x_terms, "zh", zh_size)
    along = jnp.sum(text_unit * own_terms, axis=1, keepdims=True)
    text_grad = (own_terms - text_unit * along) * text_inverse
    return (own_losses, text_grad)


def solution(mesh):
    outer = mesh.shape["dp"]
    core_size = 2
    x_size = outer // (core_size * 3)
    fine_mesh = jax.sharding.Mesh(
        mesh.devices.reshape(x_size, 3, core_size, mesh.shape["section"], mesh.shape["mp"]),
        ("x", "zh", "core", "section", "mp"),
    )
    spread = ("x", "zh", "core", "section", "mp")
    placed = (
        P(spread, None, None),
        P(),
        P(),
        P(),
        P(),
        P(spread, None),
        P(spread, None),
        P(),
        P(),
        P(),
    )
    return jax.shard_map(
        local,
        mesh=fine_mesh,
        in_specs=placed,
        out_specs=(P(spread), P(spread, None)),
        check_vma=False,
    )
```

```python
import math

import jax
import jax.numpy as jnp
from jax import lax
from jax.sharding import PartitionSpec as P

HEADS = 16
HD = 72


def pool_image(
    patch_rows, probe_request_heads, lookup_projection, content_projection, final_projection
):
    width = lookup_projection.shape[0]
    head_of_column = jnp.arange(width, dtype=jnp.int32) // HD
    probe_blocks = jnp.where(
        head_of_column[:, None] == jnp.arange(HEADS, dtype=jnp.int32)[None, :],
        probe_request_heads[:, None],
        jnp.zeros((), probe_request_heads.dtype),
    )
    key_probe = jnp.dot(lookup_projection, probe_blocks, preferred_element_type=jnp.float32)
    key_probe = (key_probe / math.sqrt(HD)).astype(jnp.bfloat16)
    scores = jnp.dot(patch_rows, key_probe, preferred_element_type=jnp.float32)
    highest = jnp.max(scores, axis=0, keepdims=True)
    exponent = jnp.exp(scores - highest)
    weights = (exponent / jnp.sum(exponent, axis=0, keepdims=True)).astype(jnp.bfloat16)
    pooled_patch = lax.dot_general(
        weights, patch_rows, (((0,), (0,)), ((), ())), preferred_element_type=jnp.float32
    ).astype(jnp.bfloat16)
    every_head = jnp.dot(pooled_patch, content_projection, preferred_element_type=jnp.float32)
    values = jnp.sum(
        every_head.reshape(HEADS, HEADS, HD)
        * jnp.eye(HEADS, dtype=jnp.float32)[:, :, None],
        axis=1,
    )
    values = values.astype(jnp.bfloat16).reshape(1, width)
    return jnp.dot(values, final_projection, preferred_element_type=jnp.float32).astype(
        jnp.bfloat16
    )


def normalize_rows(rows_in):
    widened = rows_in.astype(jnp.float32)
    inverse = lax.rsqrt(jnp.sum(widened * widened, axis=1, keepdims=True) + 1e-06)
    return (widened * inverse, inverse)


def block_contributions(
    picture_tile,
    target_tile,
    device_portion_count,
    overall_column_indices,
    score_scaling,
    starting_position,
):
    pair_scores = (
        score_scaling
        * lax.dot_general(
            picture_tile,
            device_portion_count,
            (((1,), (1,)), ((), ())),
            preferred_element_type=jnp.float32,
        )
        + starting_position
    )
    matching_flag = target_tile[:, None] == overall_column_indices[None, :]
    row_losses = jnp.sum(
        jax.nn.softplus(jnp.where(matching_flag, -pair_scores, pair_scores)), axis=1
    )
    sigmoid_derivatives = (
        (jax.nn.sigmoid(pair_scores) - matching_flag.astype(jnp.float32)) * score_scaling
    ).astype(jnp.bfloat16)
    grad_terms = lax.dot_general(
        sigmoid_derivatives,
        picture_tile,
        (((0,), (0,)), ((), ())),
        preferred_element_type=jnp.float32,
    )
    return (row_losses, grad_terms)


def shift_ring(x, axis, size, step):
    return lax.ppermute(x, axis, [(i, (i + step) % size) for i in range(size)])


def ring_gather(x, axis, size, held=None, held_step=0):
    forward, backward = x, x
    arrived = {0: x}
    forward_steps = size // 2
    backward_steps = size - 1 - forward_steps
    for step in range(1, forward_steps + 1):
        forward = shift_ring(forward, axis, size, 1)
        arrived[(size - step) % size] = forward
        if held is not None and step == held_step:
            arrived[(size - step) % size], held = lax.optimization_barrier((forward, held))
        if step <= backward_steps:
            backward = shift_ring(backward, axis, size, -1)
            arrived[step] = backward
    tile = jnp.concatenate([arrived[d] for d in range(size)], axis=0)
    return tile if held is None else (tile, held)


def direct_scatter(x, axis, size):
    pos = lax.axis_index(axis)
    blocks = x.reshape(size, x.shape[0] // size, *x.shape[1:])
    total = lax.dynamic_index_in_dim(blocks, pos, 0, keepdims=False)
    for step in range(1, size):
        outgoing = lax.dynamic_index_in_dim(blocks, (pos + step) % size, 0, keepdims=False)
        total = total + shift_ring(outgoing, axis, size, step)
    return total


def local(
    patch_features_window,
    probe_request_heads,
    lookup_projection,
    content_projection,
    final_projection,
    prior_picture_entries,
    caption_features,
    partner_indices,
    score_scale_param,
    score_shift,
):
    row_count = caption_features.shape[0]
    prior_count = prior_picture_entries.shape[0]
    section_size = lax.axis_size("section")
    mp_size = lax.axis_size("mp")
    inner_size = section_size * mp_size
    section_pos = lax.axis_index("section")
    mp_pos = lax.axis_index("mp")
    inner_pos = section_pos * mp_size + mp_pos
    outer_pos = lax.axis_index(("x", "zh", "core"))
    x_size, zh_size, core_size = lax.axis_size("x"), lax.axis_size("zh"), lax.axis_size("core")
    outer_size = x_size * zh_size * core_size
    score_scaling = score_scale_param[0]
    starting_position = score_shift[0]

    text_unit, text_inverse = normalize_rows(caption_features)
    caption_magnitude = text_unit.astype(jnp.bfloat16)
    device_portion_count = lax.all_gather(caption_magnitude, ("x", "zh", "core"), axis=0, tiled=True)

    chunk_rows = row_count
    prior_norm = normalize_rows(
        jnp.pad(prior_picture_entries, ((0, chunk_rows - prior_count), (0, 0)))
    )[0].astype(jnp.bfloat16)
    prior_tile, device_portion_count = ring_gather(
        ring_gather(prior_norm, "mp", mp_size),
        "section",
        section_size,
        held=device_portion_count,
        held_step=section_size // 2 - 1,
    )

    pooled = pool_image(
        patch_features_window[0],
        probe_request_heads,
        lookup_projection,
        content_projection,
        final_projection,
    )
    pooled_norm = normalize_rows(pooled)[0].astype(jnp.bfloat16)
    pooled_tile = lax.all_to_all(
        jnp.broadcast_to(pooled_norm, (inner_size, pooled_norm.shape[1])),
        ("section", "mp"),
        0,
        0,
        tiled=True,
    )
    picture_tile = jnp.concatenate([prior_tile, pooled_tile], axis=0)

    group_labels = lax.dynamic_slice_in_dim(
        partner_indices, outer_pos * (inner_size * row_count), inner_size * row_count
    ).reshape(section_size, mp_size, row_count)
    ring_labels = jnp.roll(jnp.roll(group_labels, -section_pos, axis=0), -mp_pos, axis=1)
    prior_labels = jnp.concatenate(
        [
            ring_labels[:, :, 1 : 1 + prior_count],
            jnp.full((section_size, mp_size, chunk_rows - prior_count), -1, jnp.int32),
        ],
        axis=2,
    ).reshape(-1)
    pooled_labels = group_labels[:, :, 0].reshape(-1)
    target_tile = jnp.concatenate([prior_labels, pooled_labels])

    width = device_portion_count.shape[1]
    device_portion_count = (
        device_portion_count.reshape(x_size, zh_size, core_size, row_count, width)
        .transpose(2, 0, 1, 3, 4)
        .reshape(outer_size * row_count, width)
    )
    blocks = jnp.arange(outer_size, dtype=jnp.int32)
    block_core = blocks // (x_size * zh_size)
    block_x = blocks // zh_size % x_size
    block_zh = blocks % zh_size
    block_dp = block_x * (zh_size * core_size) + block_zh * core_size + block_core
    overall_column_indices = (
        (block_dp * inner_size + inner_pos)[:, None] * row_count
        + jnp.arange(row_count, dtype=jnp.int32)[None, :]
    ).reshape(-1)

    row_losses, grad_terms = block_contributions(
        picture_tile,
        target_tile,
        device_portion_count,
        overall_column_indices,
        score_scaling,
        starting_position,
    )
    prior_losses = row_losses[: inner_size * chunk_rows].reshape(section_size, mp_size, chunk_rows)
    prior_losses = jnp.roll(jnp.roll(prior_losses, section_pos, axis=0), mp_pos, axis=1)
    pooled_losses = row_losses[inner_size * chunk_rows :]
    loss_parts = jnp.concatenate(
        [pooled_losses[:, None], prior_losses.reshape(inner_size, chunk_rows)[:, :prior_count]],
        axis=1,
    )
    core_terms = direct_scatter(grad_terms, "core", core_size)
    loss_parts, core_terms = lax.optimization_barrier((loss_parts, core_terms))
    section_losses = jnp.sum(
        lax.all_to_all(
            loss_parts.reshape(section_size, mp_size, row_count), "mp", 1, 1, tiled=True
        ),
        axis=1,
    )
    x_terms = direct_scatter(core_terms, "x", x_size)
    section_losses, x_terms = lax.optimization_barrier((section_losses, x_terms))
    own_losses = jnp.sum(lax.all_to_all(section_losses, "section", 0, 0, tiled=True), axis=0)
    own_terms = direct_scatter(x_terms, "zh", zh_size)
    along = jnp.sum(text_unit * own_terms, axis=1, keepdims=True)
    text_grad = (own_terms - text_unit * along) * text_inverse
    return (own_losses, text_grad)


def solution(mesh):
    outer = mesh.shape["dp"]
    core_size = 2
    x_size = outer // (core_size * 3)
    fine_mesh = jax.sharding.Mesh(
        mesh.devices.reshape(x_size, 3, core_size, mesh.shape["section"], mesh.shape["mp"]),
        ("x", "zh", "core", "section", "mp"),
    )
    spread = ("x", "zh", "core", "section", "mp")
    placed = (
        P(spread, None, None),
        P(),
        P(),
        P(),
        P(),
        P(spread, None),
        P(spread, None),
        P(),
        P(),
        P(),
    )
    return jax.shard_map(
        local,
        mesh=fine_mesh,
        in_specs=placed,
        out_specs=(P(spread), P(spread, None)),
        check_vma=False,
    )
```
